256 devices in a mesh: grp: 32 (over z, y_hi, core), tp: 8 (over y_lo, x).
Axes of the slice: x: 4, y: 4 (y_hi: 2, y_lo: 2; y = y_hi * 2 + y_lo), z: 8, core: 2. Of those that a mesh axis runs over, the one named last changes fastest.
Arguments:
- states_in: bfloat16 [16384, 1536], P('grp', 'tp'), may hold values from -6 to 6
- segment_ids: int32 [16384], P('grp'), may hold values from 0 to 223, as said below
- positions: int32 [16384], P('grp'), may hold values from 0 to 1009, as said below
- attention_gain: bfloat16 [1536], P('tp'), may hold values from 0.5 to 1.5
- feedforward_gain: bfloat16 [1536], P('tp'), may hold values from 0.5 to 1.5
- query_weight: bfloat16 [1536, 1536], P('grp', 'tp'), may hold values from -1 to 1
- keyvalue_weight: bfloat16 [1536, 8, 128], P('grp', 'tp'), may hold values from -128 to 128
- output_weight: bfloat16 [1536, 1536], P('tp'), may hold values from -0.15625 to 0.15625
- route_experts: int32 [16384, 8], P('grp'), may hold values from 0 to 19, all different within a row; in each aligned block of 512 rows (0 to 511, 512 to 1023, ...) at most 256 rows name the same one
- route_weights: float32 [16384, 8], P('grp'), may hold values from 0.05 to 0.3
- expert_gateup: bfloat16 [40, 1536, 512], P('tp'), may hold values from -0.15625 to 0.15625
- expert_down: bfloat16 [40, 256, 1536], P('tp'), may hold values from -0.25 to 0.25
- cache_slots: int32 [16384], P('grp'), may hold values from 0 to 16383, as said below
Outputs:
- layer_output: bfloat16 [16384, 1536], P('grp', 'tp')
- paged_cache: bfloat16 [16384, 8, 128], P('grp', 'tp')
- log_sums: float32 [24, 16384], P('tp', 'grp')
The draws below stay inside these ranges and needn't reach their ends.
Inputs may be any that keep to these rules, and one draw needn't show every extreme that they name: `segment_ids`: equal ids mark the tokens of one prompt; the tokens of a prompt lie within one pair of groups 2p and 2p+1. `positions`: positions count from 0 within each prompt; one prompt of groups 0 and 1 has 2 * (505) tokens. `route_experts`: each row names 8 different experts; at most 256 rows of one group name the same expert, and that number is reached. `cache_slots`: every cache row is named once; the tokens of each group fill exactly 16 rows of every group's block of 512 rows.
All inputs are finite; a program needn't handle non-finite values.
Results may differ from the reference program's by a relative error of at most 0.01.
The reference program's roundings to bfloat16 on the way count: a program that leaves them out, or rounds other values in their place, can miss the bound.
Values may be sent and summed in bfloat16 or wider, within the bound.
No kernel may reach another device: no remote copies, remote signals or barrier semaphores. Data moves between devices by JAX's collectives and lax.ppermute only.
A program may use at most 128 MiB of HBM per device.

```python
import math
import jax
import jax.numpy as jnp
import numpy as np
from jax import lax

D = 1536
QH = 24
KVH = 8
HD = 64
F = 512
TOP = 8
EXPERTS = 20
CUTS = 7
TOK_GRP = 512
TOKENS = 16384
CAP = 256
FH = 256
E_SLOT = 5
N_GRP = 32
N_TP = 8


def pack_layout(key):
    groups = TOKENS // TOK_GRP
    group_keys = jax.random.split(jax.random.fold_in(key, 7), groups)

    def cut_points(one_key):
        picks = jax.random.permutation(one_key, TOK_GRP - 1)[:CUTS] + 1
        return jnp.sort(picks.astype(jnp.int32))
    cuts = jax.vmap(cut_points)(group_keys)
    steps_row = jnp.arange(CUTS, dtype=jnp.int32)
    cuts = cuts.at[0].set(steps_row + 1)
    cuts = cuts.at[1].set(steps_row + (TOK_GRP - CUTS))
    offsets = jnp.arange(TOK_GRP, dtype=jnp.int32)
    local = jnp.sum((offsets[None, :, None] >= cuts[:, None, :]).astype(jnp.int32), axis=-1)
    starts = jnp.concatenate([jnp.zeros((groups, 1), jnp.int32), cuts], axis=1)
    finish = jnp.concatenate([cuts, jnp.full((groups, 1), TOK_GRP, jnp.int32)], axis=1)
    lengths = finish - starts
    start_of = jnp.take_along_axis(starts, local, axis=1)
    within = offsets[None, :] - start_of
    group_index = jnp.arange(groups, dtype=jnp.int32)
    partner_last = lengths[group_index ^ 1, CUTS]
    placed = jnp.where(local == 0, within + partner_last[:, None], within)
    parity = group_index % 2
    base_id = group_index // 2 * 2 * CUTS
    second_ids = jnp.where(local == 0, CUTS, jnp.where(local == CUTS, 0, CUTS + local))
    prompt_ids = base_id[:, None] + jnp.where(parity[:, None] == 0, local, second_ids)
    return (prompt_ids.reshape(-1).astype(jnp.int32), placed.reshape(-1).astype(jnp.int32))


def draw_segment_ids(key, part):
    return pack_layout(key)[0]


def draw_positions(key, part):
    return pack_layout(key)[1]


def attention_weights(key):
    query_key, key_key, value_key = jax.random.split(jax.random.fold_in(key, 11), 3)
    spread = D ** (-0.5)
    query_part = jnp.clip(jax.random.normal(query_key, (D, QH * HD), jnp.float32), -6.0, 6.0) * spread
    key_part = jnp.clip(jax.random.normal(key_key, (D, KVH, HD), jnp.float32), -6.0, 6.0) * spread
    value_part = jnp.clip(jax.random.normal(value_key, (D, KVH, HD), jnp.float32), -6.0, 6.0) * spread
    return (query_part, jnp.concatenate([key_part, value_part], axis=-1))


def draw_query_weight(key, part):
    return attention_weights(key)[0].astype(jnp.bfloat16)


def draw_keyvalue_weight(key, part):
    return attention_weights(key)[1].astype(jnp.bfloat16)


def draw_cache_slots(key, part):
    groups = TOKENS // TOK_GRP
    per_owner = TOK_GRP // groups
    source_key, owner_key = jax.random.split(jax.random.fold_in(key, 13), 2)

    def shuffled(one_key):
        return jax.random.permutation(one_key, TOK_GRP).astype(jnp.int32)
    source_order = jax.vmap(shuffled)(jax.random.split(source_key, groups))
    owner_order = jax.vmap(shuffled)(jax.random.split(owner_key, groups))
    place = jnp.arange(TOK_GRP, dtype=jnp.int32)
    owner = place // per_owner
    inner = place % per_owner
    source = jnp.arange(groups, dtype=jnp.int32)[:, None]
    local_slot = owner_order[owner[None, :], source * per_owner + inner[None, :]]
    slot_value = owner[None, :] * TOK_GRP + local_slot
    slots = jnp.zeros((groups, TOK_GRP), jnp.int32).at[source, source_order].set(slot_value)
    return slots.reshape(-1)


def level_of(stream_key, shape, cuts, low, high):
    level, own = 1.0, jax.random.fold_in(stream_key, 6)
    for dim, blocks in cuts:
        steps = jnp.exp(jax.random.uniform(jax.random.fold_in(own, dim), (blocks,), jnp.float32, low / len(cuts), high / len(cuts)))
        level = level * jnp.repeat(steps, shape[dim] // blocks).reshape([-1 if axis == dim else 1 for axis in range(len(shape))])
    return level


def routed_block(rng, own, number, rows, amount, top, limit, slope):
    sequence = jax.random.permutation(rng, amount)
    packed, common = shares(amount, rows * top, limit, slope, True), shares(amount, rows * top, limit, slope, False)
    places = jnp.arange(amount)

    def named(sizes, offset_by):
        used = int((sizes > 0).sum())
        fixed = max(1, used // 4)
        moved = fixed + (places - fixed + offset_by * (used - fixed)) % max(1, amount - fixed)
        return jnp.zeros((amount,), jnp.int32).at[sequence[jnp.where(places < fixed, places, moved)]].set(jnp.asarray(sizes, jnp.int32))

    sizes = jnp.where(number % 4 == 0, named(packed, number // 4), named(common, number - number // 4 - 1))
    mixed = jax.random.permutation(jax.random.fold_in(own, 3), amount)
    donor, sink = mixed[0:amount // 2 * 2:2], mixed[1:amount // 2 * 2:2]
    margin = jnp.minimum(sizes[donor] - 1, limit - sizes[sink]) // 2
    margin = jnp.where((donor == sequence[0]) | (sink == sequence[0]) | (sizes[sink] == 0), 0, jnp.maximum(margin, 0))
    moved = jax.random.randint(jax.random.fold_in(own, 4), (amount // 2,), 0, 1 << 20) % (margin + 1)
    sizes = sizes.at[donor].add(-moved).at[sink].add(moved)
    labels = jnp.searchsorted(jnp.cumsum(sizes), jnp.arange(rows * top), side="right").astype(jnp.int32)
    grid = labels.reshape(top, rows).T
    grid = grid[jax.random.permutation(jax.random.fold_in(own, 1), rows)]
    offset_by = jax.random.randint(jax.random.fold_in(own, 2), (rows, 1), 0, top)
    return jnp.take_along_axis(grid, (jnp.arange(top)[None, :] + offset_by) % top, axis=1)


def shares(amount, total, limit, lean, full):
    loads = [(1 << 20) // math.isqrt(grade ** lean) + 1 for grade in range(1, amount + 1)]
    largest = limit if full else min(limit, max(-(-total // amount), total * loads[0] // sum(loads)))
    least = 1 if total - largest >= amount - 1 else 0
    given, surplus = [largest] + [least] * (amount - 1), total - largest - least * (amount - 1)
    while surplus > 0:
        free = [i for i in range(1, amount) if given[i] < largest] or [i for i in range(1, amount) if given[i] < limit]
        whole, remaining = sum([loads[i] for i in free]), surplus
        for i in free:
            more = min(limit - given[i], max(1, remaining * loads[i] // whole), surplus)
            given[i] = given[i] + more
            surplus = surplus - more
    return np.array(given)


def gaussian(rng, shape, deviation, reach, cuts=(), kind=jnp.bfloat16):
    drawn = jax.random.normal(rng, shape, jnp.float32) * deviation
    if len(cuts) > 0:
        drawn = level_of(rng, shape, cuts, -0.22, 0.18) * drawn
    return jnp.clip(drawn, min=-reach, max=reach).astype(kind)


def setup_inputs(seed: int = 0) -> dict:
    key_list = jax.random.split(jax.random.key(seed), 14)
    states_in = gaussian(key_list[0], (TOKENS, D), 1.0, 6.0, ((0, 32), (1, 8)))
    segment_ids = draw_segment_ids(jax.random.fold_in(key_list[13], 71), 0)
    positions = draw_positions(jax.random.fold_in(key_list[13], 71), 0)
    attention_gain = jnp.clip(1.0 + 0.1 * jax.random.normal(key_list[3], (D,), jnp.float32), 0.5, 1.5).astype(jnp.bfloat16)
    feedforward_gain = jnp.clip(1.0 + 0.1 * jax.random.normal(key_list[4], (D,), jnp.float32), 0.5, 1.5).astype(jnp.bfloat16)
    query_weight = draw_query_weight(jax.random.fold_in(key_list[13], 71), 0)
    keyvalue_weight = draw_keyvalue_weight(jax.random.fold_in(key_list[13], 71), 0)
    output_weight = gaussian(key_list[7], (QH * HD, D), (QH * HD) ** -0.5, 0.15625, ((0, 8),))
    route_experts_keys = jax.random.split(jax.random.fold_in(key_list[8], 1), TOKENS // TOK_GRP)
    route_experts_turns = jax.random.permutation(jax.random.fold_in(key_list[8], 3), TOKENS // TOK_GRP)
    route_experts = jax.vmap(lambda own, number: routed_block(jax.random.fold_in(key_list[8], 2), own, number, TOK_GRP, EXPERTS, TOP, CAP, 1))(route_experts_keys, route_experts_turns).reshape((TOKENS, TOP))
    route_weights = jnp.clip(0.05 + 0.25 * jax.random.uniform(key_list[9], (TOKENS, TOP), jnp.float32) ** level_of(key_list[9], (TOKENS, TOP), ((0, 32),), -0.2, 0.2), 0.05, 0.3)
    expert_gateup = gaussian(key_list[10], (2 * EXPERTS, D, 2 * FH), D ** -0.5, 0.15625, ((0, 8),))
    expert_down = gaussian(key_list[11], (2 * EXPERTS, FH, D), F ** -0.5, 0.25, ((0, 8),))
    cache_slots = draw_cache_slots(jax.random.fold_in(key_list[13], 71), 0)
    return dict(states_in=states_in, segment_ids=segment_ids, positions=positions, attention_gain=attention_gain, feedforward_gain=feedforward_gain, query_weight=query_weight, keyvalue_weight=keyvalue_weight, output_weight=output_weight, route_experts=route_experts, route_weights=route_weights, expert_gateup=expert_gateup, expert_down=expert_down, cache_slots=cache_slots)


attn_scale = 0.015625
norm_eps = 1e-06
rope_base = 10000.0

def rms_scale(values, gain_row):
    floats = values.astype(jnp.float32)
    mean_square = lax.optimization_barrier(jnp.mean(floats * floats, axis=-1, keepdims=True))
    return (floats * lax.rsqrt(mean_square + norm_eps) * gain_row.astype(jnp.float32)).astype(jnp.bfloat16)

def rotate(values, places):
    half_width = values.shape[-1] // 2
    frequency = rope_base ** (-jnp.arange(half_width, dtype=jnp.float32) * 2.0 / values.shape[-1])
    angles = places.astype(jnp.float32)[:, None] * frequency[None, :]
    cosine = jnp.cos(angles)[:, None, :]
    sine_part = jnp.sin(angles)[:, None, :]
    leading = values[..., :half_width]
    trailing = values[..., half_width:]
    return jnp.concatenate([leading * cosine - trailing * sine_part, trailing * cosine + leading * sine_part], axis=-1)

def pair_attention(queries, key_rows, value_rows, segment_ids, positions, pair_index):
    pair_span = 2 * TOK_GRP
    first_row = (pair_index * pair_span).astype(jnp.int32)
    query_part = lax.dynamic_slice_in_dim(queries, first_row, pair_span, 0).astype(jnp.float32)
    query_part = query_part.reshape(pair_span, KVH, QH // KVH, HD)
    key_part = lax.dynamic_slice_in_dim(key_rows, first_row, pair_span, 0).astype(jnp.float32)
    value_part = lax.dynamic_slice_in_dim(value_rows, first_row, pair_span, 0).astype(jnp.float32)
    seg_part = lax.dynamic_slice_in_dim(segment_ids, first_row, pair_span, 0)
    pos_part = lax.dynamic_slice_in_dim(positions, first_row, pair_span, 0)
    scores = jnp.einsum('qgrd,kgd->grqk', query_part, key_part) * attn_scale
    allowed = (seg_part[:, None] == seg_part[None, :]) & (pos_part[None, :] <= pos_part[:, None])
    masked = jnp.where(allowed, scores, -jnp.inf)
    row_peak = lax.optimization_barrier(jnp.max(masked, axis=-1, keepdims=True))
    exponent = jnp.exp(masked - row_peak)
    row_total = lax.optimization_barrier(jnp.sum(exponent, axis=-1, keepdims=True))
    log_total = (row_peak + jnp.log(row_total))[..., 0].reshape(QH, pair_span)
    weights_low = lax.optimization_barrier((exponent / row_total).astype(jnp.bfloat16))
    mixed_rows = jnp.einsum('grqk,kgd->qgrd', weights_low.astype(jnp.float32), value_part)
    return (mixed_rows.astype(jnp.bfloat16).reshape(pair_span, QH * HD), log_total)

def reference(states_in, segment_ids, positions, attention_gain, feedforward_gain, query_weight, keyvalue_weight, output_weight, route_experts, route_weights, expert_gateup, expert_down, cache_slots):
    tokens = states_in.shape[0]
    normed_in = rms_scale(states_in, attention_gain)
    query_full = jnp.dot(normed_in, query_weight, preferred_element_type=jnp.float32).reshape(tokens, QH, HD)
    queries = rotate(query_full, positions).astype(jnp.bfloat16)
    keyvalue_full = jnp.dot(normed_in, keyvalue_weight.reshape(D, KVH * 2 * HD), preferred_element_type=jnp.float32)
    keyvalue_full = keyvalue_full.reshape(tokens, KVH, 2 * HD)
    key_rows = rotate(keyvalue_full[..., :HD], positions).astype(jnp.bfloat16)
    value_rows = keyvalue_full[..., HD:].astype(jnp.bfloat16)

    def one_pair(pair_index):
        return pair_attention(queries, key_rows, value_rows, segment_ids, positions, pair_index)
    mixed_all, log_all = lax.map(one_pair, jnp.arange(N_GRP // 2, dtype=jnp.int32))
    attended = mixed_all.reshape(tokens, QH * HD)
    log_sums = jnp.transpose(log_all, (1, 0, 2)).reshape(QH, tokens)
    residual = (states_in.astype(jnp.float32) + jnp.dot(attended, output_weight, preferred_element_type=jnp.float32)).astype(jnp.bfloat16)
    normed_mid = rms_scale(residual, feedforward_gain)
    gateup_split = expert_gateup.reshape(N_TP // 2, 2, E_SLOT, D, 2 * FH)
    down_split = expert_down.reshape(N_TP // 2, 2, E_SLOT, FH, D)
    groups = tokens // TOK_GRP
    routes_grouped = route_experts.reshape(groups, TOK_GRP, TOP)
    weights_grouped = route_weights.reshape(groups, TOK_GRP, TOP)
    offsets = jnp.arange(TOK_GRP, dtype=jnp.int32)
    group_base = (jnp.arange(groups, dtype=jnp.int32) * TOK_GRP)[:, None]

    def expert_step(running, expert):
        slot_index = expert // E_SLOT
        inner = expert % E_SLOT
        gateup_pair = gateup_split[slot_index, :, inner]
        down_pair = down_split[slot_index, :, inner]
        matches = routes_grouped == expert
        chosen = jnp.any(matches, axis=-1)
        route_scale = lax.optimization_barrier(jnp.sum(jnp.where(matches, weights_grouped, 0.0), axis=-1))
        ranking = jnp.argsort(jnp.where(chosen, offsets[None, :], TOK_GRP + offsets[None, :]), axis=-1)[:, :CAP]
        flat_rows = (group_base + ranking).reshape(-1).astype(jnp.int32)
        picked = normed_mid[flat_rows]
        produced = jnp.zeros((flat_rows.shape[0], D), jnp.float32)
        for half_index in range(2):
            gate_up = jnp.dot(picked, gateup_pair[half_index], preferred_element_type=jnp.float32)
            activated = (jax.nn.silu(gate_up[:, :FH]) * gate_up[:, FH:]).astype(jnp.bfloat16)
            produced = produced + jnp.dot(activated, down_pair[half_index], preferred_element_type=jnp.float32)
        scales = jnp.take_along_axis(route_scale, ranking, axis=1).reshape(-1, 1)
        running = running.at[flat_rows].add(scales * produced)
        return (running, None)
    expert_total, _ = lax.scan(expert_step, jnp.zeros((tokens, D), jnp.float32), jnp.arange(EXPERTS, dtype=jnp.int32))
    layer_output = (residual.astype(jnp.float32) + expert_total).astype(jnp.bfloat16)
    cache_content = jnp.concatenate([key_rows, value_rows], axis=-1)
    paged_cache = jnp.zeros_like(cache_content).at[cache_slots].set(cache_content)
    return (layer_output, paged_cache, log_sums)
```

```python
import jax
import jax.numpy as jnp
from jax import lax
from jax.sharding import Mesh
from jax.sharding import PartitionSpec as P

HD = 64

attn_scale = 0.015625
norm_eps = 1e-06
rope_base = 10000.0

G = ("z", "yh", "c")
T = ("yl", "x")


def rms_scale(values, gain_row):
    floats = values.astype(jnp.float32)
    mean_square = jnp.mean(floats * floats, axis=-1, keepdims=True)
    return (floats * lax.rsqrt(mean_square + norm_eps) * gain_row.astype(jnp.float32)).astype(
        jnp.bfloat16
    )


def rotate(values, places):
    half_width = values.shape[-1] // 2
    frequency = rope_base ** (-jnp.arange(half_width, dtype=jnp.float32) * 2.0 / values.shape[-1])
    angles = places.astype(jnp.float32)[:, None] * frequency[None, :]
    cosine = jnp.cos(angles)[:, None, :]
    sine_part = jnp.sin(angles)[:, None, :]
    leading = values[..., :half_width]
    trailing = values[..., half_width:]
    return jnp.concatenate(
        [leading * cosine - trailing * sine_part, trailing * cosine + leading * sine_part], axis=-1
    )


def attend_block(query_block, seg_block, pos_block, all_rows, all_seg, all_pos):
    key_part = all_rows[..., :HD]
    value_part = all_rows[..., HD:]
    scores = (
        jnp.einsum("qgrd,kgd->grqk", query_block, key_part, preferred_element_type=jnp.float32)
        * attn_scale
    )
    allowed = (seg_block[:, None] == all_seg[None, :]) & (all_pos[None, :] <= pos_block[:, None])
    masked = jnp.where(allowed, scores, -jnp.inf)
    row_peak = jnp.max(masked, axis=-1, keepdims=True)
    exponent = jnp.exp(masked - row_peak)
    row_total = jnp.sum(exponent, axis=-1, keepdims=True)
    log_total = (row_peak + jnp.log(row_total))[..., 0]
    weights_low = (exponent / row_total).astype(jnp.bfloat16)
    mixed_rows = jnp.einsum(
        "grqk,kgd->qgrd", weights_low, value_part, preferred_element_type=jnp.float32
    )
    return (mixed_rows.astype(jnp.bfloat16), log_total)


def expert_terms(normed, route_experts, route_weights, gateup, down, slot_first):
    local_experts = gateup.shape[0]
    half_units = down.shape[1]
    owned_experts = slot_first + jnp.arange(local_experts, dtype=jnp.int32)
    matches = route_experts[:, :, None] == owned_experts[None, None, :]
    route_scale = jnp.sum(jnp.where(matches, route_weights[:, :, None], 0.0), axis=1)
    gate_up = jnp.einsum("td,edf->etf", normed, gateup, preferred_element_type=jnp.float32)
    activated = (jax.nn.silu(gate_up[..., :half_units]) * gate_up[..., half_units:]).astype(
        jnp.bfloat16
    )
    produced = jnp.einsum("etf,efd->etd", activated, down, preferred_element_type=jnp.float32)
    return jnp.sum(route_scale.T[:, :, None] * produced, axis=0)


def gather_rows_over_groups(block):
    width = block.shape[1]
    nz = lax.axis_size("z")
    zi = lax.axis_index("z")
    got = [block]
    for k in range(1, nz):
        got.append(lax.ppermute(block, "z", [(i, (i + k) % nz) for i in range(nz)]))
    stacked = jnp.stack(got)
    zfull = jnp.take(stacked, (zi - jnp.arange(nz)) % nz, axis=0)
    yi = lax.axis_index("yh")
    other_y = lax.ppermute(zfull, "yh", [(0, 1), (1, 0)])
    yfull = jnp.where(yi == 0, jnp.stack([zfull, other_y]), jnp.stack([other_y, zfull]))
    ci = lax.axis_index("c")
    other_c = lax.ppermute(yfull, "c", [(0, 1), (1, 0)])
    cfull = jnp.where(ci == 0, jnp.stack([yfull, other_c]), jnp.stack([other_c, yfull]))
    return cfull.transpose(2, 1, 0, 3, 4).reshape(-1, width)


def shards(
    states_in,
    segment_ids,
    positions,
    attention_gain,
    feedforward_gain,
    query_weight,
    keyvalue_weight,
    output_weight,
    route_experts,
    route_weights,
    expert_gateup,
    expert_down,
    cache_slots,
):
    tokens = states_in.shape[0]
    width_share = states_in.shape[1]
    head_rank = lax.axis_index(T)
    group_rank = lax.axis_index(G)
    gain_rows = jnp.zeros((8, width_share), states_in.dtype)
    gain_rows = gain_rows.at[0].set(attention_gain).at[1].set(feedforward_gain)
    packed = jnp.concatenate([states_in, gain_rows], axis=0)
    packed_full = lax.all_gather(packed, T, axis=1, tiled=True)
    states_full = packed_full[:tokens]
    gain_attend = packed_full[tokens]
    gain_forward = packed_full[tokens + 1]
    normed_in = rms_scale(states_full, gain_attend)
    query_cols = query_weight.shape[1]
    keyvalue_heads = keyvalue_weight.shape[1]
    heads_local = query_cols // HD
    piece_rows = query_weight.shape[0]
    weights_packed = jnp.concatenate(
        [query_weight, keyvalue_weight.reshape(piece_rows, -1)], axis=1
    )
    weights_full = gather_rows_over_groups(weights_packed)
    query_full_w = weights_full[:, :query_cols]
    keyvalue_full_w = weights_full[:, query_cols:]
    query_sum = jnp.dot(normed_in, query_full_w, preferred_element_type=jnp.float32)
    keyvalue_sum = jnp.dot(normed_in, keyvalue_full_w, preferred_element_type=jnp.float32)
    queries = rotate(query_sum.reshape(tokens, heads_local, HD), positions).astype(jnp.bfloat16)
    keyvalue_sum = keyvalue_sum.reshape(tokens, keyvalue_heads, 2 * HD)
    key_rows = rotate(keyvalue_sum[..., :HD], positions).astype(jnp.bfloat16)
    value_rows = keyvalue_sum[..., HD:].astype(jnp.bfloat16)
    own_rows = jnp.concatenate([key_rows, value_rows], axis=-1)
    other_rows, other_seg, other_pos = lax.ppermute(
        (own_rows, segment_ids, positions), "c", [(0, 1), (1, 0)]
    )
    all_rows = jnp.concatenate([own_rows, other_rows], axis=0)
    all_seg = jnp.concatenate([segment_ids, other_seg], axis=0)
    all_pos = jnp.concatenate([positions, other_pos], axis=0)
    group_ratio = heads_local // keyvalue_heads
    query_block = queries.reshape(tokens, keyvalue_heads, group_ratio, HD)
    mixed, log_part = attend_block(query_block, segment_ids, positions, all_rows, all_seg, all_pos)
    attended = mixed.reshape(tokens, heads_local * HD)
    log_sums = log_part.reshape(heads_local, tokens)
    partial_value = jnp.dot(attended, output_weight, preferred_element_type=jnp.float32)
    summed = lax.psum(partial_value, T)
    residual = (states_full.astype(jnp.float32) + summed).astype(jnp.bfloat16)
    normed = rms_scale(residual, gain_forward)
    residual_share = lax.dynamic_slice_in_dim(residual, head_rank * width_share, width_share, 1)
    slot_first = head_rank // 2 * expert_gateup.shape[0]
    terms = expert_terms(
        normed, route_experts, route_weights, expert_gateup, expert_down, slot_first
    )
    expert_share = lax.psum_scatter(
        terms.astype(jnp.bfloat16), T, scatter_dimension=1, tiled=True
    ).astype(jnp.float32)
    layer_output = (residual_share.astype(jnp.float32) + expert_share).astype(jnp.bfloat16)
    group_count = lax.axis_size(G)
    per_owner = tokens // group_count
    owners = cache_slots // tokens
    sequence = jnp.arange(tokens, dtype=jnp.int32)
    ordering = jnp.argsort(owners * tokens + sequence)
    send_rows = own_rows[ordering].reshape(group_count, per_owner, keyvalue_heads, 2 * HD)
    send_slots = cache_slots[ordering].reshape(group_count, per_owner)
    got_rows, got_slots = (
        lax.all_to_all(send_rows, G, split_axis=0, concat_axis=0, tiled=True),
        lax.all_to_all(send_slots, G, split_axis=0, concat_axis=0, tiled=True),
    )
    targets = got_slots.reshape(tokens) - group_rank * tokens
    paged_rows = (
        jnp.zeros_like(own_rows).at[targets].set(got_rows.reshape(tokens, keyvalue_heads, 2 * HD))
    )
    return (layer_output, paged_rows, log_sums)


def solution(mesh):
    fine = Mesh(mesh.devices.reshape(8, 2, 2, 2, 4), ("z", "yh", "c", "yl", "x"))
    return jax.shard_map(
        shards,
        mesh=fine,
        in_specs=(
            P(G, T),
            P(G),
            P(G),
            P(T),
            P(T),
            P(G, T),
            P(G, T, None),
            P(T, None),
            P(G, None),
            P(G, None),
            P(T, None, None),
            P(T, None, None),
            P(G),
        ),
        out_specs=(P(G, T), P(G, T, None), P(T, G)),
        check_vma=False,
    )
```

```python
import jax
import jax.numpy as jnp
from jax import lax
from jax.sharding import Mesh
from jax.sharding import PartitionSpec as P

HD = 64

attn_scale = 0.015625
norm_eps = 1e-06
rope_base = 10000.0

G = ("z", "yh", "c")
T = ("yl", "x")


def rms_scale(values, gain_row):
    floats = values.astype(jnp.float32)
    mean_square = jnp.mean(floats * floats, axis=-1, keepdims=True)
    return (floats * lax.rsqrt(mean_square + norm_eps) * gain_row.astype(jnp.float32)).astype(
        jnp.bfloat16
    )


def rotate(values, places):
    half_width = values.shape[-1] // 2
    frequency = rope_base ** (-jnp.arange(half_width, dtype=jnp.float32) * 2.0 / values.shape[-1])
    angles = places.astype(jnp.float32)[:, None] * frequency[None, :]
    cosine = jnp.cos(angles)[:, None, :]
    sine_part = jnp.sin(angles)[:, None, :]
    leading = values[..., :half_width]
    trailing = values[..., half_width:]
    return jnp.concatenate(
        [leading * cosine - trailing * sine_part, trailing * cosine + leading * sine_part], axis=-1
    )


def attend_block(query_block, seg_block, pos_block, all_rows, all_seg, all_pos):
    key_part = all_rows[..., :HD]
    value_part = all_rows[..., HD:]
    scores = (
        jnp.einsum("qgrd,kgd->grqk", query_block, key_part, preferred_element_type=jnp.float32)
        * attn_scale
    )
    allowed = (seg_block[:, None] == all_seg[None, :]) & (all_pos[None, :] <= pos_block[:, None])
    masked = jnp.where(allowed, scores, -jnp.inf)
    row_peak = jnp.max(masked, axis=-1, keepdims=True)
    exponent = jnp.exp(masked - row_peak)
    row_total = jnp.sum(exponent, axis=-1, keepdims=True)
    log_total = (row_peak + jnp.log(row_total))[..., 0]
    weights_low = (exponent / row_total).astype(jnp.bfloat16)
    mixed_rows = jnp.einsum(
        "grqk,kgd->qgrd", weights_low, value_part, preferred_element_type=jnp.float32
    )
    return (mixed_rows.astype(jnp.bfloat16), log_total)


def expert_terms(normed, route_experts, route_weights, gateup, down, slot_first):
    local_experts = gateup.shape[0]
    half_units = down.shape[1]
    owned_experts = slot_first + jnp.arange(local_experts, dtype=jnp.int32)
    matches = route_experts[:, :, None] == owned_experts[None, None, :]
    route_scale = jnp.sum(jnp.where(matches, route_weights[:, :, None], 0.0), axis=1)
    gate_up = jnp.einsum("td,edf->etf", normed, gateup, preferred_element_type=jnp.float32)
    activated = (jax.nn.silu(gate_up[..., :half_units]) * gate_up[..., half_units:]).astype(
        jnp.bfloat16
    )
    produced = jnp.einsum("etf,efd->etd", activated, down, preferred_element_type=jnp.float32)
    return jnp.sum(route_scale.T[:, :, None] * produced, axis=0)


def gather_rows_over_groups(block):
    width = block.shape[1]
    nz = lax.axis_size("z")
    zi = lax.axis_index("z")
    got = [block]
    for k in range(1, nz):
        got.append(lax.ppermute(block, "z", [(i, (i + k) % nz) for i in range(nz)]))
    stacked = jnp.stack(got)
    zfull = jnp.take(stacked, (zi - jnp.arange(nz)) % nz, axis=0)
    yi = lax.axis_index("yh")
    other_y = lax.ppermute(zfull, "yh", [(0, 1), (1, 0)])
    yfull = jnp.where(yi == 0, jnp.stack([zfull, other_y]), jnp.stack([other_y, zfull]))
    ci = lax.axis_index("c")
    other_c = lax.ppermute(yfull, "c", [(0, 1), (1, 0)])
    cfull = jnp.where(ci == 0, jnp.stack([yfull, other_c]), jnp.stack([other_c, yfull]))
    return cfull.transpose(2, 1, 0, 3, 4).reshape(-1, width)


def place_cache_rows(own_rows, cache_slots, group_rank):
    tokens, keyvalue_heads, row_width = own_rows.shape
    group_count = lax.axis_size(G)
    per_owner = tokens // group_count
    owners = cache_slots // tokens
    sequence = jnp.arange(tokens, dtype=jnp.int32)
    ordering = jnp.argsort(owners * tokens + sequence)
    send_rows = own_rows[ordering].reshape(group_count, per_owner, keyvalue_heads, row_width)
    send_slots = cache_slots[ordering].reshape(group_count, per_owner)
    got_rows, got_slots = (
        lax.all_to_all(send_rows, G, split_axis=0, concat_axis=0, tiled=True),
        lax.all_to_all(send_slots, G, split_axis=0, concat_axis=0, tiled=True),
    )
    targets = got_slots.reshape(tokens) - group_rank * tokens
    return jnp.zeros_like(own_rows).at[targets].set(
        got_rows.reshape(tokens, keyvalue_heads, row_width)
    )


def shards(
    states_in,
    segment_ids,
    positions,
    attention_gain,
    feedforward_gain,
    query_weight,
    keyvalue_weight,
    output_weight,
    route_experts,
    route_weights,
    expert_gateup,
    expert_down,
    cache_slots,
):
    tokens = states_in.shape[0]
    width_share = states_in.shape[1]
    head_rank = lax.axis_index(T)
    group_rank = lax.axis_index(G)
    gain_rows = jnp.zeros((8, width_share), states_in.dtype)
    gain_rows = gain_rows.at[0].set(attention_gain).at[1].set(feedforward_gain)
    packed = jnp.concatenate([states_in, gain_rows], axis=0)
    packed_full = lax.all_gather(packed, T, axis=1, tiled=True)
    states_full = packed_full[:tokens]
    gain_attend = packed_full[tokens]
    gain_forward = packed_full[tokens + 1]
    normed_in = rms_scale(states_full, gain_attend)
    query_cols = query_weight.shape[1]
    keyvalue_heads = keyvalue_weight.shape[1]
    heads_local = query_cols // HD
    piece_rows = query_weight.shape[0]
    weights_packed = jnp.concatenate(
        [query_weight, keyvalue_weight.reshape(piece_rows, -1)], axis=1
    )
    weights_full = gather_rows_over_groups(weights_packed)
    query_full_w = weights_full[:, :query_cols]
    keyvalue_full_w = weights_full[:, query_cols:]
    query_sum = jnp.dot(normed_in, query_full_w, preferred_element_type=jnp.float32)
    keyvalue_sum = jnp.dot(normed_in, keyvalue_full_w, preferred_element_type=jnp.float32)
    queries = rotate(query_sum.reshape(tokens, heads_local, HD), positions).astype(jnp.bfloat16)
    keyvalue_sum = keyvalue_sum.reshape(tokens, keyvalue_heads, 2 * HD)
    key_rows = rotate(keyvalue_sum[..., :HD], positions).astype(jnp.bfloat16)
    value_rows = keyvalue_sum[..., HD:].astype(jnp.bfloat16)
    own_rows = jnp.concatenate([key_rows, value_rows], axis=-1)
    other_rows, other_seg, other_pos = lax.ppermute(
        (own_rows, segment_ids, positions), "c", [(0, 1), (1, 0)]
    )
    all_rows = jnp.concatenate([own_rows, other_rows], axis=0)
    all_seg = jnp.concatenate([segment_ids, other_seg], axis=0)
    all_pos = jnp.concatenate([positions, other_pos], axis=0)
    group_ratio = heads_local // keyvalue_heads
    query_block = queries.reshape(tokens, keyvalue_heads, group_ratio, HD)
    mixed, log_part = attend_block(query_block, segment_ids, positions, all_rows, all_seg, all_pos)
    attended = mixed.reshape(tokens, heads_local * HD)
    log_sums = log_part.reshape(heads_local, tokens)
    partial_value = jnp.dot(attended, output_weight, preferred_element_type=jnp.float32)
    partial_low, own_rows, cache_slots = lax.optimization_barrier(
        (partial_value.astype(jnp.bfloat16), own_rows, cache_slots)
    )
    summed = lax.psum(partial_low, T)
    paged_rows = place_cache_rows(own_rows, cache_slots, group_rank)
    summed, paged_rows = lax.optimization_barrier((summed, paged_rows))
    residual = (states_full.astype(jnp.float32) + summed.astype(jnp.float32)).astype(jnp.bfloat16)
    normed = rms_scale(residual, gain_forward)
    residual_share = lax.dynamic_slice_in_dim(residual, head_rank * width_share, width_share, 1)
    slot_first = head_rank // 2 * expert_gateup.shape[0]
    terms = expert_terms(
        normed, route_experts, route_weights, expert_gateup, expert_down, slot_first
    )
    expert_share = lax.psum_scatter(
        terms.astype(jnp.bfloat16), T, scatter_dimension=1, tiled=True
    ).astype(jnp.float32)
    layer_output = (residual_share.astype(jnp.float32) + expert_share).astype(jnp.bfloat16)
    return (layer_output, paged_rows, log_sums)


def solution(mesh):
    fine = Mesh(mesh.devices.reshape(8, 2, 2, 2, 4), ("z", "yh", "c", "yl", "x"))
    return jax.shard_map(
        shards,
        mesh=fine,
        in_specs=(
            P(G, T),
            P(G),
            P(G),
            P(T),
            P(T),
            P(G, T),
            P(G, T, None),
            P(T, None),
            P(G, None),
            P(G, None),
            P(T, None, None),
            P(T, None, None),
            P(G),
        ),
        out_specs=(P(G, T), P(G, T, None), P(T, G)),
        check_vma=False,
    )
```

```python
import jax
import jax.numpy as jnp
from jax import lax
from jax.sharding import Mesh
from jax.sharding import PartitionSpec as P

HD = 64

attn_scale = 0.015625
norm_eps = 1e-06
rope_base = 10000.0

G = ("z", "yh", "c")
T = ("yl", "x")


def rms_scale(values, gain_row):
    floats = values.astype(jnp.float32)
    mean_square = jnp.mean(floats * floats, axis=-1, keepdims=True)
    return (floats * lax.rsqrt(mean_square + norm_eps) * gain_row.astype(jnp.float32)).astype(
        jnp.bfloat16
    )


def rotate(values, places):
    half_width = values.shape[-1] // 2
    frequency = rope_base ** (-jnp.arange(half_width, dtype=jnp.float32) * 2.0 / values.shape[-1])
    angles = places.astype(jnp.float32)[:, None] * frequency[None, :]
    cosine = jnp.cos(angles)[:, None, :]
    sine_part = jnp.sin(angles)[:, None, :]
    leading = values[..., :half_width]
    trailing = values[..., half_width:]
    return jnp.concatenate(
        [leading * cosine - trailing * sine_part, trailing * cosine + leading * sine_part], axis=-1
    )


def attend_block(query_block, seg_block, pos_block, all_rows, all_seg, all_pos):
    key_part = all_rows[..., :HD]
    value_part = all_rows[..., HD:]
    scores = (
        jnp.einsum("qgrd,kgd->grqk", query_block, key_part, preferred_element_type=jnp.float32)
        * attn_scale
    )
    allowed = (seg_block[:, None] == all_seg[None, :]) & (all_pos[None, :] <= pos_block[:, None])
    masked = jnp.where(allowed, scores, -jnp.inf)
    row_peak = jnp.max(masked, axis=-1, keepdims=True)
    exponent = jnp.exp(masked - row_peak)
    row_total = jnp.sum(exponent, axis=-1, keepdims=True)
    log_total = (row_peak + jnp.log(row_total))[..., 0]
    weights_low = (exponent / row_total).astype(jnp.bfloat16)
    mixed_rows = jnp.einsum(
        "grqk,kgd->qgrd", weights_low, value_part, preferred_element_type=jnp.float32
    )
    return (mixed_rows.astype(jnp.bfloat16), log_total)


def expert_terms(normed, route_experts, route_weights, gateup, down, slot_first):
    local_experts = gateup.shape[0]
    half_units = down.shape[1]
    owned_experts = slot_first + jnp.arange(local_experts, dtype=jnp.int32)
    matches = route_experts[:, :, None] == owned_experts[None, None, :]
    route_scale = jnp.sum(jnp.where(matches, route_weights[:, :, None], 0.0), axis=1)
    gate_up = jnp.einsum("td,edf->etf", normed, gateup, preferred_element_type=jnp.float32)
    activated = (jax.nn.silu(gate_up[..., :half_units]) * gate_up[..., half_units:]).astype(
        jnp.bfloat16
    )
    produced = jnp.einsum("etf,efd->etd", activated, down, preferred_element_type=jnp.float32)
    return jnp.sum(route_scale.T[:, :, None] * produced, axis=0)


def gather_rows_over_groups(block):
    width = block.shape[1]
    nz = lax.axis_size("z")
    zi = lax.axis_index("z")
    got = [block]
    for k in range(1, nz):
        got.append(lax.ppermute(block, "z", [(i, (i + k) % nz) for i in range(nz)]))
    stacked = jnp.stack(got)
    zfull = jnp.take(stacked, (zi - jnp.arange(nz)) % nz, axis=0)
    yi = lax.axis_index("yh")
    other_y = lax.ppermute(zfull, "yh", [(0, 1), (1, 0)])
    yfull = jnp.where(yi == 0, jnp.stack([zfull, other_y]), jnp.stack([other_y, zfull]))
    ci = lax.axis_index("c")
    other_c = lax.ppermute(yfull, "c", [(0, 1), (1, 0)])
    cfull = jnp.where(ci == 0, jnp.stack([yfull, other_c]), jnp.stack([other_c, yfull]))
    return cfull.transpose(2, 1, 0, 3, 4).reshape(-1, width)


def place_cache_rows(own_rows, cache_slots, group_rank):
    tokens, keyvalue_heads, row_width = own_rows.shape
    group_count = lax.axis_size(G)
    per_owner = tokens // group_count
    owners = cache_slots // tokens
    sequence = jnp.arange(tokens, dtype=jnp.int32)
    ordering = jnp.argsort(owners * tokens + sequence)
    send_rows = own_rows[ordering].reshape(group_count, per_owner, keyvalue_heads, row_width)
    send_slots = cache_slots[ordering].reshape(group_count, per_owner)
    got_rows, got_slots = (
        lax.all_to_all(send_rows, G, split_axis=0, concat_axis=0, tiled=True),
        lax.all_to_all(send_slots, G, split_axis=0, concat_axis=0, tiled=True),
    )
    targets = got_slots.reshape(tokens) - group_rank * tokens
    return jnp.zeros_like(own_rows).at[targets].set(
        got_rows.reshape(tokens, keyvalue_heads, row_width)
    )


def gather_rows_over_heads(block):
    width = block.shape[1]
    nt = lax.axis_size(T)
    ti = lax.axis_index(T)
    ci = lax.axis_index("c")
    half = block.shape[0] // 2
    mine = lax.dynamic_slice_in_dim(block, ci * half, half, 0)
    got = [mine]
    for k in range(1, nt):
        got.append(lax.ppermute(mine, T, [(i, (i + k) % nt) for i in range(nt)]))
    stacked = jnp.stack(got)
    halves = jnp.take(stacked, (ti - jnp.arange(nt)) % nt, axis=0)
    other_c = lax.ppermute(halves, "c", [(0, 1), (1, 0)])
    full = jnp.where(ci == 0, jnp.stack([halves, other_c], axis=1), jnp.stack([other_c, halves], axis=1))
    return full.reshape(-1, width)


def shards(
    states_in,
    segment_ids,
    positions,
    attention_gain,
    feedforward_gain,
    query_weight,
    keyvalue_weight,
    output_weight,
    route_experts,
    route_weights,
    expert_gateup,
    expert_down,
    cache_slots,
):
    tokens = states_in.shape[0]
    width_share = states_in.shape[1]
    head_rank = lax.axis_index(T)
    group_rank = lax.axis_index(G)
    gain_rows = jnp.zeros((8, width_share), states_in.dtype)
    gain_rows = gain_rows.at[0].set(attention_gain).at[1].set(feedforward_gain)
    packed = jnp.concatenate([states_in, gain_rows], axis=0)
    packed_full = lax.all_gather(packed, T, axis=1, tiled=True)
    states_full = packed_full[:tokens]
    gain_attend = packed_full[tokens]
    gain_forward = packed_full[tokens + 1]
    normed_in = rms_scale(states_full, gain_attend)
    query_cols = query_weight.shape[1]
    keyvalue_heads = keyvalue_weight.shape[1]
    heads_local = query_cols // HD
    piece_rows = query_weight.shape[0]
    weights_packed = jnp.concatenate(
        [query_weight, keyvalue_weight.reshape(piece_rows, -1)], axis=1
    )
    weights_full = gather_rows_over_groups(weights_packed)
    output_full = gather_rows_over_heads(output_weight)
    query_full_w = weights_full[:, :query_cols]
    keyvalue_full_w = weights_full[:, query_cols:]
    query_sum = jnp.dot(normed_in, query_full_w, preferred_element_type=jnp.float32)
    keyvalue_sum = jnp.dot(normed_in, keyvalue_full_w, preferred_element_type=jnp.float32)
    queries = rotate(query_sum.reshape(tokens, heads_local, HD), positions).astype(jnp.bfloat16)
    keyvalue_sum = keyvalue_sum.reshape(tokens, keyvalue_heads, 2 * HD)
    key_rows = rotate(keyvalue_sum[..., :HD], positions).astype(jnp.bfloat16)
    value_rows = keyvalue_sum[..., HD:].astype(jnp.bfloat16)
    own_rows = jnp.concatenate([key_rows, value_rows], axis=-1)
    other_rows, other_seg, other_pos = lax.ppermute(
        (own_rows, segment_ids, positions), "c", [(0, 1), (1, 0)]
    )
    all_rows = jnp.concatenate([own_rows, other_rows], axis=0)
    all_seg = jnp.concatenate([segment_ids, other_seg], axis=0)
    all_pos = jnp.concatenate([positions, other_pos], axis=0)
    group_ratio = heads_local // keyvalue_heads
    query_block = queries.reshape(tokens, keyvalue_heads, group_ratio, HD)
    mixed, log_part = attend_block(query_block, segment_ids, positions, all_rows, all_seg, all_pos)
    attended = mixed.reshape(tokens, heads_local * HD)
    log_sums = log_part.reshape(heads_local, tokens)
    attended, own_rows, cache_slots = lax.optimization_barrier((attended, own_rows, cache_slots))
    attended_full = lax.all_gather(attended, T, axis=1, tiled=True)
    paged_rows = place_cache_rows(own_rows, cache_slots, group_rank)
    attended_full, paged_rows = lax.optimization_barrier((attended_full, paged_rows))
    mixed_out = jnp.dot(attended_full, output_full, preferred_element_type=jnp.float32)
    residual = (states_full.astype(jnp.float32) + mixed_out).astype(jnp.bfloat16)
    normed = rms_scale(residual, gain_forward)
    residual_share = lax.dynamic_slice_in_dim(residual, head_rank * width_share, width_share, 1)
    slot_first = head_rank // 2 * expert_gateup.shape[0]
    terms = expert_terms(
        normed, route_experts, route_weights, expert_gateup, expert_down, slot_first
    )
    expert_share = lax.psum_scatter(
        terms.astype(jnp.bfloat16), T, scatter_dimension=1, tiled=True
    ).astype(jnp.float32)
    layer_output = (residual_share.astype(jnp.float32) + expert_share).astype(jnp.bfloat16)
    return (layer_output, paged_rows, log_sums)


def solution(mesh):
    fine = Mesh(mesh.devices.reshape(8, 2, 2, 2, 4), ("z", "yh", "c", "yl", "x"))
    return jax.shard_map(
        shards,
        mesh=fine,
        in_specs=(
            P(G, T),
            P(G),
            P(G),
            P(T),
            P(T),
            P(G, T),
            P(G, T, None),
            P(T, None),
            P(G, None),
            P(G, None),
            P(T, None, None),
            P(T, None, None),
            P(G),
        ),
        out_specs=(P(G, T), P(G, T, None), P(T, G)),
        check_vma=False,
    )
```

```python
import jax
import jax.numpy as jnp
from jax import lax
from jax.sharding import Mesh
from jax.sharding import PartitionSpec as P

HD = 64

attn_scale = 0.015625
norm_eps = 1e-06
rope_base = 10000.0

G = ("z", "yh", "c")
T = ("yl", "x")


def rms_scale(values, gain_row):
    floats = values.astype(jnp.float32)
    mean_square = jnp.mean(floats * floats, axis=-1, keepdims=True)
    return (floats * lax.rsqrt(mean_square + norm_eps) * gain_row.astype(jnp.float32)).astype(
        jnp.bfloat16
    )


def rotate(values, places):
    half_width = values.shape[-1] // 2
    frequency = rope_base ** (-jnp.arange(half_width, dtype=jnp.float32) * 2.0 / values.shape[-1])
    angles = places.astype(jnp.float32)[:, None] * frequency[None, :]
    cosine = jnp.cos(angles)[:, None, :]
    sine_part = jnp.sin(angles)[:, None, :]
    leading = values[..., :half_width]
    trailing = values[..., half_width:]
    return jnp.concatenate(
        [leading * cosine - trailing * sine_part, trailing * cosine + leading * sine_part], axis=-1
    )


def attend_block(query_block, seg_block, pos_block, all_rows, all_seg, all_pos):
    key_part = all_rows[..., :HD]
    value_part = all_rows[..., HD:]
    scores = (
        jnp.einsum("qgrd,kgd->grqk", query_block, key_part, preferred_element_type=jnp.float32)
        * attn_scale
    )
    allowed = (seg_block[:, None] == all_seg[None, :]) & (all_pos[None, :] <= pos_block[:, None])
    masked = jnp.where(allowed, scores, -jnp.inf)
    row_peak = jnp.max(masked, axis=-1, keepdims=True)
    exponent = jnp.exp(masked - row_peak)
    row_total = jnp.sum(exponent, axis=-1, keepdims=True)
    log_total = (row_peak + jnp.log(row_total))[..., 0]
    weights_low = (exponent / row_total).astype(jnp.bfloat16)
    mixed_rows = jnp.einsum(
        "grqk,kgd->qgrd", weights_low, value_part, preferred_element_type=jnp.float32
    )
    return (mixed_rows.astype(jnp.bfloat16), log_total)


def expert_terms(normed, route_experts, route_weights, gateup, down, slot_first):
    local_experts = gateup.shape[0]
    half_units = down.shape[1]
    owned_experts = slot_first + jnp.arange(local_experts, dtype=jnp.int32)
    matches = route_experts[:, :, None] == owned_experts[None, None, :]
    route_scale = jnp.sum(jnp.where(matches, route_weights[:, :, None], 0.0), axis=1)
    gate_up = jnp.einsum("td,edf->etf", normed, gateup, preferred_element_type=jnp.float32)
    activated = (jax.nn.silu(gate_up[..., :half_units]) * gate_up[..., half_units:]).astype(
        jnp.bfloat16
    )
    produced = jnp.einsum("etf,efd->etd", activated, down, preferred_element_type=jnp.float32)
    return jnp.sum(route_scale.T[:, :, None] * produced, axis=0)


def gather_rows_over_groups(block):
    width = block.shape[1]
    nz = lax.axis_size("z")
    zi = lax.axis_index("z")
    got = [block]
    for k in range(1, nz):
        got.append(lax.ppermute(block, "z", [(i, (i + k) % nz) for i in range(nz)]))
    stacked = jnp.stack(got)
    zfull = jnp.take(stacked, (zi - jnp.arange(nz)) % nz, axis=0)
    yi = lax.axis_index("yh")
    other_y = lax.ppermute(zfull, "yh", [(0, 1), (1, 0)])
    yfull = jnp.where(yi == 0, jnp.stack([zfull, other_y]), jnp.stack([other_y, zfull]))
    ci = lax.axis_index("c")
    other_c = lax.ppermute(yfull, "c", [(0, 1), (1, 0)])
    cfull = jnp.where(ci == 0, jnp.stack([yfull, other_c]), jnp.stack([other_c, yfull]))
    return cfull.transpose(2, 1, 0, 3, 4).reshape(-1, width)


def place_cache_rows(own_rows, cache_slots, group_rank):
    tokens, keyvalue_heads, row_width = own_rows.shape
    group_count = lax.axis_size(G)
    per_owner = tokens // group_count
    owners = cache_slots // tokens
    sequence = jnp.arange(tokens, dtype=jnp.int32)
    ordering = jnp.argsort(owners * tokens + sequence)
    send_rows = own_rows[ordering].reshape(group_count, per_owner, keyvalue_heads, row_width)
    send_slots = cache_slots[ordering].reshape(group_count, per_owner)
    got_rows, got_slots = (
        lax.all_to_all(send_rows, G, split_axis=0, concat_axis=0, tiled=True),
        lax.all_to_all(send_slots, G, split_axis=0, concat_axis=0, tiled=True),
    )
    targets = got_slots.reshape(tokens) - group_rank * tokens
    return jnp.zeros_like(own_rows).at[targets].set(
        got_rows.reshape(tokens, keyvalue_heads, row_width)
    )


def shards(
    states_in,
    segment_ids,
    positions,
    attention_gain,
    feedforward_gain,
    query_weight,
    keyvalue_weight,
    output_weight,
    route_experts,
    route_weights,
    expert_gateup,
    expert_down,
    cache_slots,
):
    tokens = states_in.shape[0]
    width_share = states_in.shape[1]
    head_rank = lax.axis_index(T)
    group_rank = lax.axis_index(G)
    gain_rows = jnp.zeros((8, width_share), states_in.dtype)
    gain_rows = gain_rows.at[0].set(attention_gain).at[1].set(feedforward_gain)
    packed = jnp.concatenate([states_in, gain_rows], axis=0)
    packed_full = lax.all_gather(packed, T, axis=1, tiled=True)
    states_full = packed_full[:tokens]
    gain_attend = packed_full[tokens]
    gain_forward = packed_full[tokens + 1]
    normed_in = rms_scale(states_full, gain_attend)
    query_cols = query_weight.shape[1]
    keyvalue_heads = keyvalue_weight.shape[1]
    heads_local = query_cols // HD
    piece_rows = query_weight.shape[0]
    weights_packed = jnp.concatenate(
        [query_weight, keyvalue_weight.reshape(piece_rows, -1)], axis=1
    )
    weights_full = gather_rows_over_groups(weights_packed)
    query_full_w = weights_full[:, :query_cols]
    keyvalue_full_w = weights_full[:, query_cols:]
    query_sum = jnp.dot(normed_in, query_full_w, preferred_element_type=jnp.float32)
    keyvalue_sum = jnp.dot(normed_in, keyvalue_full_w, preferred_element_type=jnp.float32)
    queries = rotate(query_sum.reshape(tokens, heads_local, HD), positions).astype(jnp.bfloat16)
    keyvalue_sum = keyvalue_sum.reshape(tokens, keyvalue_heads, 2 * HD)
    key_rows = rotate(keyvalue_sum[..., :HD], positions).astype(jnp.bfloat16)
    value_rows = keyvalue_sum[..., HD:].astype(jnp.bfloat16)
    own_rows = jnp.concatenate([key_rows, value_rows], axis=-1)
    other_rows, other_seg, other_pos = lax.ppermute(
        (own_rows, segment_ids, positions), "c", [(0, 1), (1, 0)]
    )
    all_rows = jnp.concatenate([own_rows, other_rows], axis=0)
    all_seg = jnp.concatenate([segment_ids, other_seg], axis=0)
    all_pos = jnp.concatenate([positions, other_pos], axis=0)
    group_ratio = heads_local // keyvalue_heads
    query_block = queries.reshape(tokens, keyvalue_heads, group_ratio, HD)
    mixed, log_part = attend_block(query_block, segment_ids, positions, all_rows, all_seg, all_pos)
    attended = mixed.reshape(tokens, heads_local * HD)
    log_sums = log_part.reshape(heads_local, tokens)
    partial_value = jnp.dot(attended, output_weight, preferred_element_type=jnp.float32)
    tp_count = lax.axis_size(T)
    value_parts = partial_value.astype(jnp.bfloat16).reshape(tokens, tp_count, width_share).transpose(1, 0, 2)
    value_got = lax.all_to_all(value_parts, T, 0, 0, tiled=True)
    summed_share = jnp.sum(value_got.astype(jnp.float32), axis=0)
    residual_share = (states_in.astype(jnp.float32) + summed_share).astype(jnp.bfloat16)
    residual_share, own_rows, cache_slots = lax.optimization_barrier((residual_share, own_rows, cache_slots))
    residual = lax.all_gather(residual_share, T, axis=1, tiled=True)
    paged_rows = place_cache_rows(own_rows, cache_slots, group_rank)
    residual, paged_rows = lax.optimization_barrier((residual, paged_rows))
    normed = rms_scale(residual, gain_forward)
    slot_first = head_rank // 2 * expert_gateup.shape[0]
    terms = expert_terms(
        normed, route_experts, route_weights, expert_gateup, expert_down, slot_first
    )
    term_parts = terms.astype(jnp.bfloat16).reshape(tokens, tp_count, width_share).transpose(1, 0, 2)
    term_got = lax.all_to_all(term_parts, T, 0, 0, tiled=True)
    expert_share = jnp.sum(term_got.astype(jnp.float32), axis=0)
    layer_output = (residual_share.astype(jnp.float32) + expert_share).astype(jnp.bfloat16)
    return (layer_output, paged_rows, log_sums)


def solution(mesh):
    fine = Mesh(mesh.devices.reshape(8, 2, 2, 2, 4), ("z", "yh", "c", "yl", "x"))
    return jax.shard_map(
        shards,
        mesh=fine,
        in_specs=(
            P(G, T),
            P(G),
            P(G),
            P(T),
            P(T),
            P(G, T),
            P(G, T, None),
            P(T, None),
            P(G, None),
            P(G, None),
            P(T, None, None),
            P(T, None, None),
            P(G),
        ),
        out_specs=(P(G, T), P(G, T, None), P(T, G)),
        check_vma=False,
    )
```

```python
import jax
import jax.numpy as jnp
from jax import lax
from jax.sharding import Mesh
from jax.sharding import PartitionSpec as P

HD = 64

attn_scale = 0.015625
norm_eps = 1e-06
rope_base = 10000.0

G = ("z", "yh", "c")
T = ("yl", "x")


def rms_scale(values, gain_row):
    floats = values.astype(jnp.float32)
    mean_square = jnp.mean(floats * floats, axis=-1, keepdims=True)
    return (floats * lax.rsqrt(mean_square + norm_eps) * gain_row.astype(jnp.float32)).astype(
        jnp.bfloat16
    )


def rotate(values, places):
    half_width = values.shape[-1] // 2
    frequency = rope_base ** (-jnp.arange(half_width, dtype=jnp.float32) * 2.0 / values.shape[-1])
    angles = places.astype(jnp.float32)[:, None] * frequency[None, :]
    cosine = jnp.cos(angles)[:, None, :]
    sine_part = jnp.sin(angles)[:, None, :]
    leading = values[..., :half_width]
    trailing = values[..., half_width:]
    return jnp.concatenate(
        [leading * cosine - trailing * sine_part, trailing * cosine + leading * sine_part], axis=-1
    )


def attend_block(query_block, seg_block, pos_block, all_rows, all_seg, all_pos):
    key_part = all_rows[..., :HD]
    value_part = all_rows[..., HD:]
    scores = (
        jnp.einsum("qgrd,kgd->grqk", query_block, key_part, preferred_element_type=jnp.float32)
        * attn_scale
    )
    allowed = (seg_block[:, None] == all_seg[None, :]) & (all_pos[None, :] <= pos_block[:, None])
    masked = jnp.where(allowed, scores, -jnp.inf)
    row_peak = jnp.max(masked, axis=-1, keepdims=True)
    exponent = jnp.exp(masked - row_peak)
    row_total = jnp.sum(exponent, axis=-1, keepdims=True)
    log_total = (row_peak + jnp.log(row_total))[..., 0]
    weights_low = (exponent / row_total).astype(jnp.bfloat16)
    mixed_rows = jnp.einsum(
        "grqk,kgd->qgrd", weights_low, value_part, preferred_element_type=jnp.float32
    )
    return (mixed_rows.astype(jnp.bfloat16), log_total)


def expert_terms(normed, route_experts, route_weights, gateup, down, slot_first):
    local_experts = gateup.shape[0]
    half_units = down.shape[1]
    owned_experts = slot_first + jnp.arange(local_experts, dtype=jnp.int32)
    matches = route_experts[:, :, None] == owned_experts[None, None, :]
    route_scale = jnp.sum(jnp.where(matches, route_weights[:, :, None], 0.0), axis=1)
    gate_up = jnp.einsum("td,edf->etf", normed, gateup, preferred_element_type=jnp.float32)
    activated = (jax.nn.silu(gate_up[..., :half_units]) * gate_up[..., half_units:]).astype(
        jnp.bfloat16
    )
    produced = jnp.einsum("etf,efd->etd", activated, down, preferred_element_type=jnp.float32)
    return jnp.sum(route_scale.T[:, :, None] * produced, axis=0)


def gather_rows_over_groups(block):
    width = block.shape[1]
    nz = lax.axis_size("z")
    zi = lax.axis_index("z")
    got = [block]
    for k in range(1, nz):
        got.append(lax.ppermute(block, "z", [(i, (i + k) % nz) for i in range(nz)]))
    stacked = jnp.stack(got)
    zfull = jnp.take(stacked, (zi - jnp.arange(nz)) % nz, axis=0)
    yi = lax.axis_index("yh")
    other_y = lax.ppermute(zfull, "yh", [(0, 1), (1, 0)])
    yfull = jnp.where(yi == 0, jnp.stack([zfull, other_y]), jnp.stack([other_y, zfull]))
    ci = lax.axis_index("c")
    other_c = lax.ppermute(yfull, "c", [(0, 1), (1, 0)])
    cfull = jnp.where(ci == 0, jnp.stack([yfull, other_c]), jnp.stack([other_c, yfull]))
    return cfull.transpose(2, 1, 0, 3, 4).reshape(-1, width)


def place_cache_rows(own_rows, cache_slots, group_rank):
    tokens, keyvalue_heads, row_width = own_rows.shape
    width = keyvalue_heads * row_width
    group_count = lax.axis_size(G)
    per_owner = tokens // group_count
    sequence = jnp.arange(tokens, dtype=jnp.int32)
    owners = cache_slots // tokens
    owner_hot = (owners[:, None] == jnp.arange(group_count, dtype=jnp.int32)[None, :]).astype(
        jnp.bfloat16
    )
    earlier = (sequence[:, None] > sequence[None, :]).astype(jnp.bfloat16)
    before = jnp.dot(earlier, owner_hot, preferred_element_type=jnp.float32)
    rank = jnp.sum(before * owner_hot.astype(jnp.float32), axis=1).astype(jnp.int32)
    place = owners * per_owner + rank
    moving = (place[None, :] == sequence[:, None]).astype(jnp.bfloat16)
    digits = jnp.stack([cache_slots // 128, cache_slots % 128], axis=1).astype(jnp.bfloat16)
    payload = jnp.concatenate([own_rows.reshape(tokens, width), digits], axis=1)
    sent = jnp.dot(moving, payload, preferred_element_type=jnp.float32).astype(jnp.bfloat16)
    sent_rows = sent[:, :width].reshape(group_count, per_owner, width)
    sent_digits = sent[:, width:].reshape(group_count, per_owner, 2).transpose(0, 2, 1)
    digit_row = jnp.zeros((group_count, 1, width), jnp.bfloat16)
    digit_row = lax.dynamic_update_slice(
        digit_row, sent_digits.reshape(group_count, 1, 2 * per_owner), (0, 0, 0)
    )
    packet = jnp.concatenate([sent_rows, digit_row], axis=1)
    got = lax.all_to_all(packet, G, 0, 0, tiled=True)
    got_rows = got[:, :per_owner, :].reshape(tokens, width)
    got_digits = got[:, per_owner, : 2 * per_owner].astype(jnp.int32).reshape(group_count, 2, per_owner)
    got_slots = (got_digits[:, 0, :] * 128 + got_digits[:, 1, :]).reshape(tokens)
    targets = got_slots - group_rank * tokens
    landing = (targets[None, :] == sequence[:, None]).astype(jnp.bfloat16)
    placed = jnp.dot(landing, got_rows, preferred_element_type=jnp.float32).astype(jnp.bfloat16)
    return placed.reshape(tokens, keyvalue_heads, row_width)


def shards(
    states_in,
    segment_ids,
    positions,
    attention_gain,
    feedforward_gain,
    query_weight,
    keyvalue_weight,
    output_weight,
    route_experts,
    route_weights,
    expert_gateup,
    expert_down,
    cache_slots,
):
    tokens = states_in.shape[0]
    width_share = states_in.shape[1]
    head_rank = lax.axis_index(T)
    group_rank = lax.axis_index(G)
    gain_rows = jnp.zeros((8, width_share), states_in.dtype)
    gain_rows = gain_rows.at[0].set(attention_gain).at[1].set(feedforward_gain)
    packed = jnp.concatenate([states_in, gain_rows], axis=0)
    packed_full = lax.all_gather(packed, T, axis=1, tiled=True)
    states_full = packed_full[:tokens]
    gain_attend = packed_full[tokens]
    gain_forward = packed_full[tokens + 1]
    normed_in = rms_scale(states_full, gain_attend)
    query_cols = query_weight.shape[1]
    keyvalue_heads = keyvalue_weight.shape[1]
    heads_local = query_cols // HD
    piece_rows = query_weight.shape[0]
    weights_packed = jnp.concatenate(
        [query_weight, keyvalue_weight.reshape(piece_rows, -1)], axis=1
    )
    weights_full = gather_rows_over_groups(weights_packed)
    query_full_w = weights_full[:, :query_cols]
    keyvalue_full_w = weights_full[:, query_cols:]
    query_sum = jnp.dot(normed_in, query_full_w, preferred_element_type=jnp.float32)
    keyvalue_sum = jnp.dot(normed_in, keyvalue_full_w, preferred_element_type=jnp.float32)
    queries = rotate(query_sum.reshape(tokens, heads_local, HD), positions).astype(jnp.bfloat16)
    keyvalue_sum = keyvalue_sum.reshape(tokens, keyvalue_heads, 2 * HD)
    key_rows = rotate(keyvalue_sum[..., :HD], positions).astype(jnp.bfloat16)
    value_rows = keyvalue_sum[..., HD:].astype(jnp.bfloat16)
    own_rows = jnp.concatenate([key_rows, value_rows], axis=-1)
    other_rows, other_seg, other_pos = lax.ppermute(
        (own_rows, segment_ids, positions), "c", [(0, 1), (1, 0)]
    )
    all_rows = jnp.concatenate([own_rows, other_rows], axis=0)
    all_seg = jnp.concatenate([segment_ids, other_seg], axis=0)
    all_pos = jnp.concatenate([positions, other_pos], axis=0)
    group_ratio = heads_local // keyvalue_heads
    query_block = queries.reshape(tokens, keyvalue_heads, group_ratio, HD)
    mixed, log_part = attend_block(query_block, segment_ids, positions, all_rows, all_seg, all_pos)
    attended = mixed.reshape(tokens, heads_local * HD)
    log_sums = log_part.reshape(heads_local, tokens)
    partial_value = jnp.dot(attended, output_weight, preferred_element_type=jnp.float32)
    tp_count = lax.axis_size(T)
    value_parts = partial_value.astype(jnp.bfloat16).reshape(tokens, tp_count, width_share).transpose(1, 0, 2)
    value_got = lax.all_to_all(value_parts, T, 0, 0, tiled=True)
    summed_share = jnp.sum(value_got.astype(jnp.float32), axis=0)
    residual_share = (states_in.astype(jnp.float32) + summed_share).astype(jnp.bfloat16)
    residual_share, own_rows, cache_slots = lax.optimization_barrier((residual_share, own_rows, cache_slots))
    residual = lax.all_gather(residual_share, T, axis=1, tiled=True)
    paged_rows = place_cache_rows(own_rows, cache_slots, group_rank)
    residual, paged_rows = lax.optimization_barrier((residual, paged_rows))
    normed = rms_scale(residual, gain_forward)
    slot_first = head_rank // 2 * expert_gateup.shape[0]
    terms = expert_terms(
        normed, route_experts, route_weights, expert_gateup, expert_down, slot_first
    )
    term_parts = terms.astype(jnp.bfloat16).reshape(tokens, tp_count, width_share).transpose(1, 0, 2)
    term_got = lax.all_to_all(term_parts, T, 0, 0, tiled=True)
    expert_share = jnp.sum(term_got.astype(jnp.float32), axis=0)
    layer_output = (residual_share.astype(jnp.float32) + expert_share).astype(jnp.bfloat16)
    return (layer_output, paged_rows, log_sums)


def solution(mesh):
    fine = Mesh(mesh.devices.reshape(8, 2, 2, 2, 4), ("z", "yh", "c", "yl", "x"))
    return jax.shard_map(
        shards,
        mesh=fine,
        in_specs=(
            P(G, T),
            P(G),
            P(G),
            P(T),
            P(T),
            P(G, T),
            P(G, T, None),
            P(T, None),
            P(G, None),
            P(G, None),
            P(T, None, None),
            P(T, None, None),
            P(G),
        ),
        out_specs=(P(G, T), P(G, T, None), P(T, G)),
        check_vma=False,
    )
```

```python
import jax
import jax.numpy as jnp
from jax import lax
from jax.sharding import Mesh
from jax.sharding import PartitionSpec as P

HD = 64

attn_scale = 0.015625
norm_eps = 1e-06
rope_base = 10000.0

G = ("z", "yh", "c")
T = ("yl", "x")


def rms_scale(values, gain_row):
    floats = values.astype(jnp.float32)
    mean_square = jnp.mean(floats * floats, axis=-1, keepdims=True)
    return (floats * lax.rsqrt(mean_square + norm_eps) * gain_row.astype(jnp.float32)).astype(
        jnp.bfloat16
    )


def rotate(values, places):
    half_width = values.shape[-1] // 2
    frequency = rope_base ** (-jnp.arange(half_width, dtype=jnp.float32) * 2.0 / values.shape[-1])
    angles = places.astype(jnp.float32)[:, None] * frequency[None, :]
    cosine = jnp.cos(angles)[:, None, :]
    sine_part = jnp.sin(angles)[:, None, :]
    leading = values[..., :half_width]
    trailing = values[..., half_width:]
    return jnp.concatenate(
        [leading * cosine - trailing * sine_part, trailing * cosine + leading * sine_part], axis=-1
    )


def attend_block(query_block, seg_block, pos_block, all_rows, all_seg, all_pos):
    key_part = all_rows[..., :HD]
    value_part = all_rows[..., HD:]
    scores = (
        jnp.einsum("qgrd,kgd->grqk", query_block, key_part, preferred_element_type=jnp.float32)
        * attn_scale
    )
    allowed = (seg_block[:, None] == all_seg[None, :]) & (all_pos[None, :] <= pos_block[:, None])
    masked = jnp.where(allowed, scores, -jnp.inf)
    row_peak = jnp.max(masked, axis=-1, keepdims=True)
    exponent = jnp.exp(masked - row_peak)
    row_total = jnp.sum(exponent, axis=-1, keepdims=True)
    log_total = (row_peak + jnp.log(row_total))[..., 0]
    weights_low = (exponent / row_total).astype(jnp.bfloat16)
    mixed_rows = jnp.einsum(
        "grqk,kgd->qgrd", weights_low, value_part, preferred_element_type=jnp.float32
    )
    return (mixed_rows.astype(jnp.bfloat16), log_total)


def expert_terms(normed, route_experts, route_weights, gateup, down, slot_first):
    local_experts = gateup.shape[0]
    half_units = down.shape[1]
    owned_experts = slot_first + jnp.arange(local_experts, dtype=jnp.int32)
    matches = route_experts[:, :, None] == owned_experts[None, None, :]
    route_scale = jnp.sum(jnp.where(matches, route_weights[:, :, None], 0.0), axis=1)
    gate_up = jnp.einsum("td,edf->etf", normed, gateup, preferred_element_type=jnp.float32)
    activated = (jax.nn.silu(gate_up[..., :half_units]) * gate_up[..., half_units:]).astype(
        jnp.bfloat16
    )
    produced = jnp.einsum("etf,efd->etd", activated, down, preferred_element_type=jnp.float32)
    return jnp.sum(route_scale.T[:, :, None] * produced, axis=0)


def gather_rows_over_groups(block):
    width = block.shape[1]
    ci = lax.axis_index("c")
    other_c = lax.ppermute(block, "c", [(0, 1), (1, 0)])
    cfull = jnp.where(ci == 0, jnp.stack([block, other_c]), jnp.stack([other_c, block]))
    yi = lax.axis_index("yh")
    other_y = lax.ppermute(cfull, "yh", [(0, 1), (1, 0)])
    yfull = jnp.where(yi == 0, jnp.stack([cfull, other_y]), jnp.stack([other_y, cfull]))
    nz = lax.axis_size("z")
    zi = lax.axis_index("z")
    got = [yfull]
    for k in range(1, nz):
        got.append(lax.ppermute(yfull, "z", [(i, (i + k) % nz) for i in range(nz)]))
    stacked = jnp.stack(got)
    zfull = jnp.take(stacked, (zi - jnp.arange(nz)) % nz, axis=0)
    return zfull.reshape(-1, width)

def place_cache_rows(own_rows, cache_slots, group_rank):
    tokens, keyvalue_heads, row_width = own_rows.shape
    width = keyvalue_heads * row_width
    group_count = lax.axis_size(G)
    per_owner = tokens // group_count
    sequence = jnp.arange(tokens, dtype=jnp.int32)
    owners = cache_slots // tokens
    owner_hot = (owners[:, None] == jnp.arange(group_count, dtype=jnp.int32)[None, :]).astype(
        jnp.bfloat16
    )
    earlier = (sequence[:, None] > sequence[None, :]).astype(jnp.bfloat16)
    before = jnp.dot(earlier, owner_hot, preferred_element_type=jnp.float32)
    rank = jnp.sum(before * owner_hot.astype(jnp.float32), axis=1).astype(jnp.int32)
    place = owners * per_owner + rank
    moving = (place[None, :] == sequence[:, None]).astype(jnp.bfloat16)
    digits = jnp.stack([cache_slots // 128, cache_slots % 128], axis=1).astype(jnp.bfloat16)
    payload = jnp.concatenate([own_rows.reshape(tokens, width), digits], axis=1)
    sent = jnp.dot(moving, payload, preferred_element_type=jnp.float32).astype(jnp.bfloat16)
    sent_rows = sent[:, :width].reshape(group_count, per_owner, width)
    sent_digits = sent[:, width:].reshape(group_count, per_owner, 2).transpose(0, 2, 1)
    digit_row = jnp.zeros((group_count, 1, width), jnp.bfloat16)
    digit_row = lax.dynamic_update_slice(
        digit_row, sent_digits.reshape(group_count, 1, 2 * per_owner), (0, 0, 0)
    )
    packet = jnp.concatenate([sent_rows, digit_row], axis=1)
    got = lax.all_to_all(packet, G, 0, 0, tiled=True)
    got_rows = got[:, :per_owner, :].reshape(tokens, width)
    got_digits = got[:, per_owner, : 2 * per_owner].astype(jnp.int32).reshape(group_count, 2, per_owner)
    got_slots = (got_digits[:, 0, :] * 128 + got_digits[:, 1, :]).reshape(tokens)
    targets = got_slots - group_rank * tokens
    landing = (targets[None, :] == sequence[:, None]).astype(jnp.bfloat16)
    placed = jnp.dot(landing, got_rows, preferred_element_type=jnp.float32).astype(jnp.bfloat16)
    return placed.reshape(tokens, keyvalue_heads, row_width)


def shards(
    states_in,
    segment_ids,
    positions,
    attention_gain,
    feedforward_gain,
    query_weight,
    keyvalue_weight,
    output_weight,
    route_experts,
    route_weights,
    expert_gateup,
    expert_down,
    cache_slots,
):
    tokens = states_in.shape[0]
    width_share = states_in.shape[1]
    head_rank = lax.axis_index(T)
    group_rank = lax.axis_index(G)
    gain_rows = jnp.zeros((8, width_share), states_in.dtype)
    gain_rows = gain_rows.at[0].set(attention_gain).at[1].set(feedforward_gain)
    packed = jnp.concatenate([states_in, gain_rows], axis=0)
    packed_full = lax.all_gather(packed, T, axis=1, tiled=True)
    states_full = packed_full[:tokens]
    gain_attend = packed_full[tokens]
    gain_forward = packed_full[tokens + 1]
    normed_in = rms_scale(states_full, gain_attend)
    query_cols = query_weight.shape[1]
    keyvalue_heads = keyvalue_weight.shape[1]
    heads_local = query_cols // HD
    piece_rows = query_weight.shape[0]
    weights_packed = jnp.concatenate(
        [query_weight, keyvalue_weight.reshape(piece_rows, -1)], axis=1
    )
    weights_full = gather_rows_over_groups(weights_packed)
    query_full_w = weights_full[:, :query_cols]
    keyvalue_full_w = weights_full[:, query_cols:]
    query_sum = jnp.dot(normed_in, query_full_w, preferred_element_type=jnp.float32)
    keyvalue_sum = jnp.dot(normed_in, keyvalue_full_w, preferred_element_type=jnp.float32)
    queries = rotate(query_sum.reshape(tokens, heads_local, HD), positions).astype(jnp.bfloat16)
    keyvalue_sum = keyvalue_sum.reshape(tokens, keyvalue_heads, 2 * HD)
    key_rows = rotate(keyvalue_sum[..., :HD], positions).astype(jnp.bfloat16)
    value_rows = keyvalue_sum[..., HD:].astype(jnp.bfloat16)
    own_rows = jnp.concatenate([key_rows, value_rows], axis=-1)
    other_rows, other_seg, other_pos = lax.ppermute(
        (own_rows, segment_ids, positions), "c", [(0, 1), (1, 0)]
    )
    all_rows = jnp.concatenate([own_rows, other_rows], axis=0)
    all_seg = jnp.concatenate([segment_ids, other_seg], axis=0)
    all_pos = jnp.concatenate([positions, other_pos], axis=0)
    group_ratio = heads_local // keyvalue_heads
    query_block = queries.reshape(tokens, keyvalue_heads, group_ratio, HD)
    mixed, log_part = attend_block(query_block, segment_ids, positions, all_rows, all_seg, all_pos)
    attended = mixed.reshape(tokens, heads_local * HD)
    log_sums = log_part.reshape(heads_local, tokens)
    partial_value = jnp.dot(attended, output_weight, preferred_element_type=jnp.float32)
    tp_count = lax.axis_size(T)
    value_parts = partial_value.astype(jnp.bfloat16).reshape(tokens, tp_count, width_share).transpose(1, 0, 2)
    value_got = lax.all_to_all(value_parts, T, 0, 0, tiled=True)
    summed_share = jnp.sum(value_got.astype(jnp.float32), axis=0)
    residual_share = (states_in.astype(jnp.float32) + summed_share).astype(jnp.bfloat16)
    residual_share, own_rows, cache_slots = lax.optimization_barrier((residual_share, own_rows, cache_slots))
    residual = lax.all_gather(residual_share, T, axis=1, tiled=True)
    paged_rows = place_cache_rows(own_rows, cache_slots, group_rank)
    residual, paged_rows = lax.optimization_barrier((residual, paged_rows))
    normed = rms_scale(residual, gain_forward)
    slot_first = head_rank // 2 * expert_gateup.shape[0]
    terms = expert_terms(
        normed, route_experts, route_weights, expert_gateup, expert_down, slot_first
    )
    term_parts = terms.astype(jnp.bfloat16).reshape(tokens, tp_count, width_share).transpose(1, 0, 2)
    term_got = lax.all_to_all(term_parts, T, 0, 0, tiled=True)
    expert_share = jnp.sum(term_got.astype(jnp.float32), axis=0)
    layer_output = (residual_share.astype(jnp.float32) + expert_share).astype(jnp.bfloat16)
    return (layer_output, paged_rows, log_sums)


def solution(mesh):
    fine = Mesh(mesh.devices.reshape(8, 2, 2, 2, 4), ("z", "yh", "c", "yl", "x"))
    return jax.shard_map(
        shards,
        mesh=fine,
        in_specs=(
            P(G, T),
            P(G),
            P(G),
            P(T),
            P(T),
            P(G, T),
            P(G, T, None),
            P(T, None),
            P(G, None),
            P(G, None),
            P(T, None, None),
            P(T, None, None),
            P(G),
        ),
        out_specs=(P(G, T), P(G, T, None), P(T, G)),
        check_vma=False,
    )
```
